1024 devices in a mesh: section: 16 (over y, z_hi), dp: 8 (over x, core), tensor: 8 (over z_lo).
Axes of the slice: x: 4, y: 8, z: 16 (z_hi: 2, z_lo: 8; z = z_hi * 8 + z_lo), core: 2. Of those that a mesh axis runs over, the one named last changes fastest.
Arguments:
- queries: bfloat16 [16, 8192, 4096], P('section', ('dp', 'tensor')), parts along dimension 1, may hold values from -50 to 50
- keys_values: bfloat16 [16, 8192, 4, 256], P('section', ('dp', 'tensor')), parts along dimension 1, may hold values from -5 to 5
- segment_ids: int32 [16, 8192], P('section', ('dp', 'tensor')), parts along dimension 1, may hold values from 0 to 3, never falling along the last dimension, each value on 1 to 640 neighbouring positions
- bounds: int32 [16, 32], P('section', 'dp'), parts along dimension 1, may hold values from 0 to 1023
Outputs:
- received: bfloat16 [16, 8192, 4096], P('section', ('dp', 'tensor')), parts along dimension 1
The draws below stay inside these ranges and needn't reach their ends.
There are 8 independent parts, one for each index of `dp`. The reference program is written for one: setup_inputs(seed, part) draws one part's arguments, and reference() takes and returns one part's arrays. A program takes and returns all parts, laid end to end along the dimension named above; each array names one. Nothing has to cross between parts.
Inputs may be any that keep to these rules, and one draw needn't show every extreme that they name: `segment_ids`: segment numbers never fall along a micro-batch; each document has 1 to 640 tokens and one has exactly 640.
All inputs are finite; a program needn't handle non-finite values.
Results may differ from the reference program's by a relative error of at most 0.0037.
Values may be sent and summed in bfloat16 or wider, within the bound.
No kernel may reach another device: no remote copies, remote signals or barrier semaphores. Data moves between devices by JAX's collectives and lax.ppermute only.
A program may use at most 64 MiB of HBM per device.

```python
import math
import jax
import jax.numpy as jnp
import numpy as np
from jax import lax

HEAD_WIDTH = 128
QUERY_HEADS = 32
KEY_VALUE_HEADS = 4
COUNT = 4
RELAY_COUNT = 16
BATCH_TOKENS = 1024
MOST = 640


def draw_both(key):
    base_value = jnp.clip(jax.random.normal(jax.random.fold_in(key, 12), (RELAY_COUNT, BATCH_TOKENS, KEY_VALUE_HEADS, 2 * HEAD_WIDTH), jnp.float32), -5.0, 5.0)
    query_sample = jnp.clip(jax.random.normal(jax.random.fold_in(key, 11), (RELAY_COUNT, BATCH_TOKENS, KEY_VALUE_HEADS, QUERY_HEADS // KEY_VALUE_HEADS, HEAD_WIDTH), jnp.float32), -5.0, 5.0)
    return (query_sample.reshape(RELAY_COUNT, BATCH_TOKENS, QUERY_HEADS * HEAD_WIDTH), base_value)


def draw_queries(key, part):
    return draw_both(key)[0].astype(jnp.bfloat16)


def draw_keys_values(key, part):
    return draw_both(key)[1].astype(jnp.bfloat16)


def plant(entries, stream_key, smallest, high):
    longest = entries.shape.index(max(entries.shape))
    spots = []
    for shift in (0, 1):
        where = [jax.random.randint(jax.random.fold_in(stream_key, axis), (), 0, length) for axis, length in enumerate(entries.shape)]
        where[longest] = (where[longest] + shift) % entries.shape[longest]
        spots.append(tuple(where))
    return entries.at[spots[0]].set(smallest).at[spots[1]].set(high)


def split_up(count, total, most, lean):
    weights = [(1 << 20) // math.isqrt(standing ** lean) + 1 for standing in range(2, count + 1)]
    surplus, given = total - most - (count - 1), [1] * (count - 1)
    while surplus > 0:
        candidates = [i for i in range(count - 1) if given[i] < most]
        mass, left = sum([weights[i] for i in candidates]), surplus
        for i in candidates:
            more = min(most - given[i], max(1, left * weights[i] // mass), surplus)
            given[i] = given[i] + more
            surplus = surplus - more
    return np.array([most] + given)


def uneven_parts(stream_key, amount, total, reach, slope):
    if amount == 2:
        one = jax.random.randint(stream_key, (), max(1, total - reach), min(reach, total - 1) + 1)
        return jnp.stack([one, total - one])
    tallies = jnp.asarray(split_up(amount, total, reach, slope), jnp.int32)
    twos = (amount - 1) // 2
    giver, taker = tallies[1:1 + 2 * twos:2], tallies[2:2 + 2 * twos:2]
    slack = jnp.minimum(giver - 1, reach - taker)
    moved = jax.random.randint(jax.random.fold_in(stream_key, 1), (twos,), 0, 1 << 20) % (slack + 1)
    tallies = tallies.at[1:1 + 2 * twos:2].set(giver - moved).at[2:2 + 2 * twos:2].set(taker + moved)
    return tallies[jax.random.permutation(jax.random.fold_in(stream_key, 2), amount)]


def setup_inputs(seed: int = 0, part: int = 0) -> dict:
    streams_of = jax.random.split(jax.random.key(seed), 5)
    part_keys = jax.random.split(jax.random.fold_in(streams_of[4], part), 5)
    return {
        "queries": draw_queries(jax.random.fold_in(jax.random.fold_in(streams_of[4], part), 71), part),
        "keys_values": draw_keys_values(jax.random.fold_in(jax.random.fold_in(streams_of[4], part), 71), part),
        "segment_ids": jax.vmap(lambda own: jnp.searchsorted(jnp.cumsum(uneven_parts(own, COUNT, BATCH_TOKENS, MOST, 2)), jnp.arange(BATCH_TOKENS), side="right"))(jax.random.split(part_keys[2], RELAY_COUNT)).reshape((RELAY_COUNT, BATCH_TOKENS)).astype(jnp.int32),
        "bounds": plant(jax.random.randint(part_keys[3], (RELAY_COUNT, COUNT), 0, BATCH_TOKENS), jax.random.fold_in(part_keys[3], 1), 0, BATCH_TOKENS - 1).astype(jnp.int32),
    }


def attend_section(query_rows, key_values, segments, limits):
    seq = query_rows.shape[0]
    kv_heads = key_values.shape[1]
    head_size = key_values.shape[2] // 2
    groups = query_rows.shape[1] // head_size // kv_heads
    positions = jnp.arange(seq)
    query_bound = limits[segments]
    visible = (segments[:, None] == segments[None, :]) & ((positions[None, :] <= positions[:, None]) | (positions[None, :] <= query_bound[:, None]))
    shaped = query_rows.reshape(seq, kv_heads, groups, head_size)
    scale = 1.0 / math.sqrt(head_size)

    def one_group(index):
        query_part = jnp.take(shaped, index, axis=1).astype(jnp.float32)
        pair = jnp.take(key_values, index, axis=1)
        key_part = pair[:, :head_size].astype(jnp.float32)
        value_part = pair[:, head_size:].astype(jnp.float32)
        scores = jnp.einsum('rgd,nd->grn', query_part, key_part) * scale
        scores = jnp.where(visible[None], scores, -1e+30)
        largest = lax.optimization_barrier(jnp.max(scores, axis=-1, keepdims=True))
        weight = jnp.where(visible[None], jnp.exp(scores - largest), 0.0)
        total = lax.optimization_barrier(jnp.sum(weight, axis=-1))
        rounded = weight.astype(jnp.bfloat16).astype(jnp.float32)
        summed = jnp.einsum('grn,nd->rgd', rounded, value_part)
        return summed / jnp.transpose(total)[:, :, None]
    outputs = lax.map(one_group, jnp.arange(kv_heads))
    return jnp.transpose(outputs, (1, 0, 2, 3)).reshape(seq, kv_heads * groups * head_size).astype(jnp.bfloat16)

def reference(queries, keys_values, segment_ids, bounds):
    attended = lax.map(lambda items: attend_section(items[0], items[1], items[2], items[3]), (queries, keys_values, segment_ids, bounds))
    return jnp.roll(attended, 1, axis=0)
```

```python
import math

import jax
import jax.numpy as jnp
from jax import lax
from jax.sharding import PartitionSpec as P


def from_behind(block, axis, distance):
    devices = range(lax.axis_size(axis))
    route = [((i - distance) % len(devices), i) for i in devices]
    return lax.ppermute(block, axis, route)


def bound_of(segments, limits):
    levels = jnp.arange(limits.shape[0])
    return jnp.sum(jnp.where(segments[:, None] == levels[None, :], limits[None, :], 0), axis=1)


def attend(queries, keys_values, segment_ids, bounds):
    query_rows = queries[0]
    pairs = keys_values[0]
    segments = segment_ids[0]
    limits = bounds[0]
    rows = query_rows.shape[0]
    kv_heads = pairs.shape[1]
    width = pairs.shape[2]
    head_size = width // 2
    heads = query_rows.shape[1] // head_size
    groups = heads // kv_heads
    scale = 1.0 / math.sqrt(head_size)
    lane = 128
    tensor_size = lax.axis_size("tensor")
    my_first = lax.axis_index("tensor") * rows
    query_pos = my_first + jnp.arange(rows)
    query_bound = bound_of(segments, limits)
    shaped = query_rows.reshape(rows, kv_heads, groups, head_size)

    flat = pairs.reshape(rows * kv_heads * width // lane, lane)
    pad_rows = 16
    seg_block = jnp.zeros((pad_rows, lane), jnp.bfloat16)
    seg_block = seg_block.at[: rows // lane].set(segments.astype(jnp.bfloat16).reshape(rows // lane, lane))
    packed = jnp.concatenate([flat, seg_block], axis=0)
    gathered = lax.all_gather(packed, "tensor", axis=0, tiled=False)
    body_rows = flat.shape[0]
    pair_piece = gathered[:, :body_rows].reshape(tensor_size * rows, kv_heads, width)
    key_segment = gathered[:, body_rows : body_rows + rows // lane].reshape(tensor_size * rows).astype(jnp.int32)

    count = pair_piece.shape[0]
    key_pos = jnp.arange(count)
    visible = (segments[:, None] == key_segment[None, :]) & (
        (key_pos[None, :] <= query_pos[:, None]) | (key_pos[None, :] <= query_bound[:, None])
    )
    mask_bias = jnp.where(visible, 0.0, -1e30).astype(jnp.float32)

    pieces = []
    for h in range(kv_heads):
      q_h = shaped[:, h]
      k_h = pair_piece[:, h, :head_size]
      v_h = pair_piece[:, h, head_size:]
      scores = (
          jnp.einsum("rgd,nd->grn", q_h, k_h, preferred_element_type=jnp.float32) * scale
          + mask_bias[None]
      )
      largest = jnp.max(scores, axis=-1)
      weight = jnp.exp(scores - largest[..., None])
      total = jnp.sum(weight, axis=-1)
      summed = jnp.einsum(
          "grn,nd->grd", weight.astype(jnp.bfloat16), v_h, preferred_element_type=jnp.float32
      )
      out_h = (
          jnp.transpose(summed / total[..., None], (1, 0, 2))
          .reshape(rows, groups * head_size)
          .astype(jnp.bfloat16)
      )
      pieces.append(from_behind(out_h, "section", 1))
    result = jnp.concatenate(pieces, axis=1)
    return result[None]


def solution(mesh):
    in_specs = (
        P("section", ("dp", "tensor"), None),
        P("section", ("dp", "tensor"), None, None),
        P("section", ("dp", "tensor")),
        P("section", "dp"),
    )
    out_specs = P("section", ("dp", "tensor"), None)
    return jax.shard_map(attend, mesh=mesh, in_specs=in_specs, out_specs=out_specs, check_vma=False)
```

```python
import functools
import math

import jax
import jax.numpy as jnp
from jax import lax
from jax.experimental import pallas as pl
from jax.sharding import PartitionSpec as P


def from_behind(block, axis, distance):
    devices = range(lax.axis_size(axis))
    route = [((i - distance) % len(devices), i) for i in devices]
    return lax.ppermute(block, axis, route)


def bound_of(segments, limits):
    levels = jnp.arange(limits.shape[0])
    return jnp.sum(jnp.where(segments[:, None] == levels[None, :], limits[None, :], 0), axis=1)


def attention_kernel(q_ref, g_ref, b_ref, o_ref, *, groups, head_size, scale):
    h = pl.program_id(0)
    parts = g_ref.shape[0]
    span = parts * head_size
    k_at = pl.multiple_of(h * 2 * head_size, 2 * head_size)
    v_at = pl.multiple_of(h * 2 * head_size + head_size, head_size)
    k = g_ref[:, pl.ds(k_at, head_size), :].reshape(span, head_size)
    v = g_ref[:, pl.ds(v_at, head_size), :].reshape(span, head_size)
    bias = b_ref[...]
    for g in range(groups):
        qg = q_ref[:, g * head_size : (g + 1) * head_size]
        s = lax.dot_general(qg, k, (((1,), (1,)), ((), ())), preferred_element_type=jnp.float32)
        s = s * scale + bias
        m = jnp.max(s, axis=1, keepdims=True)
        w = jnp.exp(s - m)
        total = jnp.sum(w, axis=1, keepdims=True)
        pv = jnp.dot(w.astype(jnp.bfloat16), v, preferred_element_type=jnp.float32)
        o_ref[:, g * head_size : (g + 1) * head_size] = (pv / total).astype(o_ref.dtype)


def attention(q, gathered, bias, kv_heads, head_size):
    rows, width = q.shape
    groups = width // head_size // kv_heads
    block = groups * head_size
    kernel = functools.partial(
        attention_kernel, groups=groups, head_size=head_size, scale=1.0 / math.sqrt(head_size)
    )
    return pl.pallas_call(
        kernel,
        grid=(kv_heads,),
        in_specs=[
            pl.BlockSpec((rows, block), lambda h: (0, h)),
            pl.BlockSpec(gathered.shape, lambda h: (0, 0, 0)),
            pl.BlockSpec(bias.shape, lambda h: (0, 0)),
        ],
        out_specs=pl.BlockSpec((rows, block), lambda h: (0, h)),
        out_shape=jax.ShapeDtypeStruct((rows, width), jnp.bfloat16),
    )(q, gathered, bias)


def shards(queries, keys_values, segment_ids, bounds):
    query_rows = queries[0]
    pairs = keys_values[0]
    segments = segment_ids[0]
    limits = bounds[0]
    rows = query_rows.shape[0]
    kv_heads = pairs.shape[1]
    width = pairs.shape[2]
    head_size = width // 2
    lane = 128
    levels = limits.shape[0]
    tensor_size = lax.axis_size("tensor")

    body = pairs.reshape(rows, kv_heads, 2, head_size).transpose(1, 2, 0, 3).reshape(-1, head_size)
    extra = jnp.zeros((16, lane), jnp.bfloat16)
    extra = extra.at[0, :rows].set(segments.astype(jnp.bfloat16))
    extra = extra.at[1, :levels].set((limits // 32).astype(jnp.bfloat16))
    extra = extra.at[1, levels : 2 * levels].set((limits % 32).astype(jnp.bfloat16))
    packed = jnp.concatenate([body, extra], axis=0)
    body_rows = body.shape[0]

    packed_prev = from_behind(packed, "section", 1)
    query_prev = from_behind(query_rows, "section", 1)
    gathered = lax.all_gather(packed_prev, "tensor", axis=0, tiled=False)

    key_segment = gathered[:, body_rows, :rows].reshape(tensor_size * rows).astype(jnp.int32)
    own_segment = packed_prev[body_rows, :rows].astype(jnp.int32)
    halves = packed_prev[body_rows + 1].astype(jnp.int32)
    limits_prev = halves[:levels] * 32 + halves[levels : 2 * levels]

    my_first = lax.axis_index("tensor") * rows
    query_pos = my_first + jnp.arange(rows)
    query_bound = bound_of(own_segment, limits_prev)
    key_pos = jnp.arange(tensor_size * rows)
    visible = (own_segment[:, None] == key_segment[None, :]) & (
        (key_pos[None, :] <= query_pos[:, None]) | (key_pos[None, :] <= query_bound[:, None])
    )
    mask_bias = jnp.where(visible, 0.0, -1e30).astype(jnp.float32)

    result = attention(query_prev, gathered, mask_bias, kv_heads, head_size)
    return result[None]


def solution(mesh):
    in_specs = (
        P("section", ("dp", "tensor"), None),
        P("section", ("dp", "tensor"), None, None),
        P("section", ("dp", "tensor")),
        P("section", "dp"),
    )
    out_specs = P("section", ("dp", "tensor"), None)
    return jax.shard_map(shards, mesh=mesh, in_specs=in_specs, out_specs=out_specs, check_vma=False)
```

```python
import functools
import math

import jax
import jax.numpy as jnp
from jax import lax
from jax.experimental import pallas as pl
from jax.sharding import PartitionSpec as P


def from_behind(block, axis, distance):
    devices = range(lax.axis_size(axis))
    route = [((i - distance) % len(devices), i) for i in devices]
    return lax.ppermute(block, axis, route)


def bound_of(segments, limits):
    levels = jnp.arange(limits.shape[0])
    return jnp.sum(jnp.where(segments[:, None] == levels[None, :], limits[None, :], 0), axis=1)


def attention_kernel(q_ref, *refs, groups, head_size, scale):
    slot_refs, b_ref, o_ref = refs[:-2], refs[-2], refs[-1]
    h = pl.program_id(0)
    k_at = pl.multiple_of(h * 2 * head_size, 2 * head_size)
    v_at = pl.multiple_of(h * 2 * head_size + head_size, head_size)
    k = jnp.concatenate([r[pl.ds(k_at, head_size), :] for r in slot_refs], axis=0)
    v = jnp.concatenate([r[pl.ds(v_at, head_size), :] for r in slot_refs], axis=0)
    bias = b_ref[...]
    for g in range(groups):
        qg = q_ref[:, g * head_size : (g + 1) * head_size]
        s = lax.dot_general(qg, k, (((1,), (1,)), ((), ())), preferred_element_type=jnp.float32)
        s = s * scale + bias
        m = jnp.max(s, axis=1, keepdims=True)
        w = jnp.exp(s - m)
        total = jnp.sum(w, axis=1, keepdims=True)
        pv = jnp.dot(w.astype(jnp.bfloat16), v, preferred_element_type=jnp.float32)
        o_ref[:, g * head_size : (g + 1) * head_size] = (pv / total).astype(o_ref.dtype)


def attention(q, slots, bias, kv_heads, head_size):
    rows, width = q.shape
    groups = width // head_size // kv_heads
    block = groups * head_size
    kernel = functools.partial(
        attention_kernel, groups=groups, head_size=head_size, scale=1.0 / math.sqrt(head_size)
    )
    return pl.pallas_call(
        kernel,
        grid=(kv_heads,),
        in_specs=[
            pl.BlockSpec((rows, block), lambda h: (0, h)),
            *[pl.BlockSpec(x.shape, lambda h: (0, 0)) for x in slots],
            pl.BlockSpec(bias.shape, lambda h: (0, 0)),
        ],
        out_specs=pl.BlockSpec((rows, block), lambda h: (0, h)),
        out_shape=jax.ShapeDtypeStruct((rows, width), jnp.bfloat16),
    )(q, *slots, bias)


def ring_gather(x, axis):
    n = lax.axis_size(axis)
    route = [(i, (i + 1) % n) for i in range(n)]
    slots = [x]
    for k in range(1, n):
        slots.append(lax.ppermute(slots[-1], axis, route))
    return slots


def shards(queries, keys_values, segment_ids, bounds):
    query_rows = queries[0]
    pairs = keys_values[0]
    segments = segment_ids[0]
    limits = bounds[0]
    rows = query_rows.shape[0]
    kv_heads = pairs.shape[1]
    width = pairs.shape[2]
    head_size = width // 2
    lane = 128
    levels = limits.shape[0]
    tensor_size = lax.axis_size("tensor")

    body = pairs.reshape(rows, kv_heads, 2, head_size).transpose(1, 2, 0, 3).reshape(-1, head_size)
    extra = jnp.zeros((16, lane), jnp.bfloat16)
    extra = extra.at[0, :rows].set(segments.astype(jnp.bfloat16))
    extra = extra.at[1, :levels].set((limits // 32).astype(jnp.bfloat16))
    extra = extra.at[1, levels : 2 * levels].set((limits % 32).astype(jnp.bfloat16))
    packed = jnp.concatenate([body, extra], axis=0)
    body_rows = body.shape[0]

    packed_prev = from_behind(packed, "section", 1)
    query_prev = from_behind(query_rows, "section", 1)
    slots = ring_gather(packed_prev, "tensor")

    key_segment = jnp.concatenate([x[body_rows, :rows] for x in slots]).astype(jnp.int32)
    own_segment = packed_prev[body_rows, :rows].astype(jnp.int32)
    halves = packed_prev[body_rows + 1].astype(jnp.int32)
    limits_prev = halves[:levels] * 32 + halves[levels : 2 * levels]

    my_first = lax.axis_index("tensor") * rows
    query_pos = my_first + jnp.arange(rows)
    query_bound = bound_of(own_segment, limits_prev)
    me = lax.axis_index("tensor")
    key_pos = jnp.concatenate([((me - k) % tensor_size) * rows + jnp.arange(rows) for k in range(tensor_size)])
    visible = (own_segment[:, None] == key_segment[None, :]) & (
        (key_pos[None, :] <= query_pos[:, None]) | (key_pos[None, :] <= query_bound[:, None])
    )
    mask_bias = jnp.where(visible, 0.0, -1e30).astype(jnp.float32)

    result = attention(query_prev, slots, mask_bias, kv_heads, head_size)
    return result[None]


def solution(mesh):
    in_specs = (
        P("section", ("dp", "tensor"), None),
        P("section", ("dp", "tensor"), None, None),
        P("section", ("dp", "tensor")),
        P("section", "dp"),
    )
    out_specs = P("section", ("dp", "tensor"), None)
    return jax.shard_map(shards, mesh=mesh, in_specs=in_specs, out_specs=out_specs, check_vma=False)
```

```python
import functools
import math

import jax
import jax.numpy as jnp
from jax import lax
from jax.experimental import pallas as pl
from jax.sharding import PartitionSpec as P


def from_behind(block, axis, distance):
    devices = range(lax.axis_size(axis))
    route = [((i - distance) % len(devices), i) for i in devices]
    return lax.ppermute(block, axis, route)


def bound_of(segments, limits):
    levels = jnp.arange(limits.shape[0])
    return jnp.sum(jnp.where(segments[:, None] == levels[None, :], limits[None, :], 0), axis=1)


def attention_kernel(q_ref, g_ref, b_ref, o_ref, *, head, groups, head_size, scale):
    parts = g_ref.shape[0]
    span = parts * head_size
    k_at = head * 2 * head_size
    k = g_ref[:, k_at : k_at + head_size, :].reshape(span, head_size)
    v = g_ref[:, k_at + head_size : k_at + 2 * head_size, :].reshape(span, head_size)
    bias = b_ref[...]
    for g in range(groups):
        qg = q_ref[:, g * head_size : (g + 1) * head_size]
        s = lax.dot_general(qg, k, (((1,), (1,)), ((), ())), preferred_element_type=jnp.float32)
        s = s * scale + bias
        m = jnp.max(s, axis=1, keepdims=True)
        w = jnp.exp(s - m)
        total = jnp.sum(w, axis=1, keepdims=True)
        pv = jnp.dot(w.astype(jnp.bfloat16), v, preferred_element_type=jnp.float32)
        o_ref[:, g * head_size : (g + 1) * head_size] = (pv / total).astype(o_ref.dtype)


def attention_head(q, gathered, bias, head, kv_heads, head_size):
    rows, width = q.shape
    groups = width // head_size // kv_heads
    block = groups * head_size
    kernel = functools.partial(
        attention_kernel, head=head, groups=groups, head_size=head_size, scale=1.0 / math.sqrt(head_size)
    )
    return pl.pallas_call(
        kernel,
        grid=(1,),
        in_specs=[
            pl.BlockSpec((rows, block), lambda i: (0, head)),
            pl.BlockSpec(gathered.shape, lambda i: (0, 0, 0)),
            pl.BlockSpec(bias.shape, lambda i: (0, 0)),
        ],
        out_specs=pl.BlockSpec((rows, block), lambda i: (0, 0)),
        out_shape=jax.ShapeDtypeStruct((rows, block), jnp.bfloat16),
    )(q, gathered, bias)


def attend(queries, keys_values, segment_ids, bounds):
    query_rows = queries[0]
    pairs = keys_values[0]
    segments = segment_ids[0]
    limits = bounds[0]
    rows = query_rows.shape[0]
    kv_heads = pairs.shape[1]
    width = pairs.shape[2]
    head_size = width // 2
    lane = 128
    tensor_size = lax.axis_size("tensor")

    body = pairs.reshape(rows, kv_heads, 2, head_size).transpose(1, 2, 0, 3).reshape(-1, head_size)
    extra = jnp.zeros((16, lane), jnp.bfloat16)
    extra = extra.at[0, :rows].set(segments.astype(jnp.bfloat16))
    packed = jnp.concatenate([body, extra], axis=0)
    body_rows = body.shape[0]
    gathered = lax.all_gather(packed, "tensor", axis=0, tiled=False)
    key_segment = gathered[:, body_rows, :rows].reshape(tensor_size * rows).astype(jnp.int32)

    my_first = lax.axis_index("tensor") * rows
    query_pos = my_first + jnp.arange(rows)
    query_bound = bound_of(segments, limits)
    key_pos = jnp.arange(tensor_size * rows)
    visible = (segments[:, None] == key_segment[None, :]) & (
        (key_pos[None, :] <= query_pos[:, None]) | (key_pos[None, :] <= query_bound[:, None])
    )
    mask_bias = jnp.where(visible, 0.0, -1e30).astype(jnp.float32)

    pieces = []
    for h in range(kv_heads):
        out_h = attention_head(query_rows, gathered, mask_bias, h, kv_heads, head_size)
        pieces.append(from_behind(out_h, "section", 1))
    return jnp.concatenate(pieces, axis=1)[None]


def solution(mesh):
    in_specs = (
        P("section", ("dp", "tensor"), None),
        P("section", ("dp", "tensor"), None, None),
        P("section", ("dp", "tensor")),
        P("section", "dp"),
    )
    out_specs = P("section", ("dp", "tensor"), None)
    return jax.shard_map(attend, mesh=mesh, in_specs=in_specs, out_specs=out_specs, check_vma=False)
```

```python
import functools
import math

import jax
import jax.numpy as jnp
from jax import lax
from jax.experimental import pallas as pl
from jax.sharding import PartitionSpec as P


def from_behind(block, axis, distance):
    devices = range(lax.axis_size(axis))
    route = [((i - distance) % len(devices), i) for i in devices]
    return lax.ppermute(block, axis, route)


def bound_of(segments, limits):
    levels = jnp.arange(limits.shape[0])
    return jnp.sum(jnp.where(segments[:, None] == levels[None, :], limits[None, :], 0), axis=1)


def attention_kernel(q_ref, g_ref, b_ref, o_ref, *, groups, head_size, scale):
    parts = g_ref.shape[0]
    span = parts * head_size
    k = g_ref[:, :head_size, :].reshape(span, head_size)
    v = g_ref[:, head_size:, :].reshape(span, head_size)
    bias = b_ref[...]
    for g in range(groups):
        qg = q_ref[:, g * head_size : (g + 1) * head_size]
        s = lax.dot_general(qg, k, (((1,), (1,)), ((), ())), preferred_element_type=jnp.float32)
        s = s * scale + bias
        m = jnp.max(s, axis=1, keepdims=True)
        w = jnp.exp(s - m)
        total = jnp.sum(w, axis=1, keepdims=True)
        pv = jnp.dot(w.astype(jnp.bfloat16), v, preferred_element_type=jnp.float32)
        o_ref[:, g * head_size : (g + 1) * head_size] = (pv / total).astype(o_ref.dtype)


def attention_head(q, gathered, bias, head, local, kv_heads, head_size):
    rows, width = q.shape
    groups = width // head_size // kv_heads
    block = groups * head_size
    kernel = functools.partial(
        attention_kernel, groups=groups, head_size=head_size, scale=1.0 / math.sqrt(head_size)
    )
    return pl.pallas_call(
        kernel,
        grid=(1,),
        in_specs=[
            pl.BlockSpec((rows, block), lambda i: (0, head)),
            pl.BlockSpec((gathered.shape[0], 2 * head_size, gathered.shape[2]), lambda i: (0, local, 0)),
            pl.BlockSpec(bias.shape, lambda i: (0, 0)),
        ],
        out_specs=pl.BlockSpec((rows, block), lambda i: (0, 0)),
        out_shape=jax.ShapeDtypeStruct((rows, block), jnp.bfloat16),
    )(q, gathered, bias)


def attend(queries, keys_values, segment_ids, bounds):
    query_rows = queries[0]
    pairs = keys_values[0]
    segments = segment_ids[0]
    limits = bounds[0]
    rows = query_rows.shape[0]
    kv_heads = pairs.shape[1]
    width = pairs.shape[2]
    head_size = width // 2
    lane = 128
    tensor_size = lax.axis_size("tensor")

    body = pairs.reshape(rows, kv_heads, 2, head_size).transpose(1, 2, 0, 3).reshape(-1, head_size)
    half = kv_heads // 2
    half_rows = half * 2 * rows
    extra = jnp.zeros((16, lane), jnp.bfloat16)
    extra = extra.at[0, :rows].set(segments.astype(jnp.bfloat16))
    first = lax.all_gather(jnp.concatenate([body[:half_rows], extra], axis=0), "tensor", axis=0, tiled=False)
    second = lax.all_gather(body[half_rows:], "tensor", axis=0, tiled=False)
    key_segment = first[:, half_rows, :rows].reshape(tensor_size * rows).astype(jnp.int32)

    my_first = lax.axis_index("tensor") * rows
    query_pos = my_first + jnp.arange(rows)
    query_bound = bound_of(segments, limits)
    key_pos = jnp.arange(tensor_size * rows)
    visible = (segments[:, None] == key_segment[None, :]) & (
        (key_pos[None, :] <= query_pos[:, None]) | (key_pos[None, :] <= query_bound[:, None])
    )
    mask_bias = jnp.where(visible, 0.0, -1e30).astype(jnp.float32)

    pieces = []
    for h in range(kv_heads):
        source = first if h < half else second
        out_h = attention_head(query_rows, source, mask_bias, h, h % half, kv_heads, head_size)
        pieces.append(from_behind(out_h, "section", 1))
    return jnp.concatenate(pieces, axis=1)[None]


def solution(mesh):
    in_specs = (
        P("section", ("dp", "tensor"), None),
        P("section", ("dp", "tensor"), None, None),
        P("section", ("dp", "tensor")),
        P("section", "dp"),
    )
    out_specs = P("section", ("dp", "tensor"), None)
    return jax.shard_map(attend, mesh=mesh, in_specs=in_specs, out_specs=out_specs, check_vma=False)
```

```python
import functools
import math

import jax
import jax.numpy as jnp
from jax import lax
from jax.experimental import pallas as pl
from jax.sharding import PartitionSpec as P


def from_behind(block, axis, distance):
    devices = range(lax.axis_size(axis))
    route = [((i - distance) % len(devices), i) for i in devices]
    return lax.ppermute(block, axis, route)


def bound_of(segments, limits):
    levels = jnp.arange(limits.shape[0])
    return jnp.sum(jnp.where(segments[:, None] == levels[None, :], limits[None, :], 0), axis=1)


def attention_kernel(q_ref, g_ref, s_ref, i_ref, o_ref, *, groups, head_size, scale):
    parts = g_ref.shape[0]
    span = parts * head_size
    k = g_ref[:, :head_size, :].reshape(span, head_size)
    v = g_ref[:, head_size:, :].reshape(span, head_size)
    own = i_ref[:, 0:1]
    place = i_ref[:, 1:2]
    reach = i_ref[:, 2:3]
    blocks = []
    for p in range(parts):
        key_seg = s_ref[p, 0:1, :].astype(jnp.int32)
        key_pos = p * head_size + lax.broadcasted_iota(jnp.int32, (1, head_size), 1)
        seen = (own == key_seg) & ((key_pos <= place) | (key_pos <= reach))
        blocks.append(jnp.where(seen, 0.0, -1e30).astype(jnp.float32))
    bias = jnp.concatenate(blocks, axis=1)
    for g in range(groups):
        qg = q_ref[:, g * head_size : (g + 1) * head_size]
        s = lax.dot_general(qg, k, (((1,), (1,)), ((), ())), preferred_element_type=jnp.float32)
        s = s * scale + bias
        m = jnp.max(s, axis=1, keepdims=True)
        w = jnp.exp(s - m)
        total = jnp.sum(w, axis=1, keepdims=True)
        pv = jnp.dot(w.astype(jnp.bfloat16), v, preferred_element_type=jnp.float32)
        o_ref[:, g * head_size : (g + 1) * head_size] = (pv / total).astype(o_ref.dtype)


def attention_head(q, gathered, info, head, id_row, kv_heads, head_size):
    rows, width = q.shape
    groups = width // head_size // kv_heads
    block = groups * head_size
    kernel = functools.partial(
        attention_kernel, groups=groups, head_size=head_size, scale=1.0 / math.sqrt(head_size)
    )
    return pl.pallas_call(
        kernel,
        grid=(1,),
        in_specs=[
            pl.BlockSpec((rows, block), lambda i: (0, head)),
            pl.BlockSpec((gathered.shape[0], 2 * head_size, gathered.shape[2]), lambda i: (0, head, 0)),
            pl.BlockSpec((gathered.shape[0], 16, gathered.shape[2]), lambda i: (0, id_row // 16, 0)),
            pl.BlockSpec(info.shape, lambda i: (0, 0)),
        ],
        out_specs=pl.BlockSpec((rows, block), lambda i: (0, 0)),
        out_shape=jax.ShapeDtypeStruct((rows, block), jnp.bfloat16),
    )(q, gathered, gathered, info)


def attend(queries, keys_values, segment_ids, bounds):
    query_rows = queries[0]
    pairs = keys_values[0]
    segments = segment_ids[0]
    limits = bounds[0]
    rows = query_rows.shape[0]
    kv_heads = pairs.shape[1]
    width = pairs.shape[2]
    head_size = width // 2
    lane = 128

    body = pairs.reshape(rows, kv_heads, 2, head_size).transpose(1, 2, 0, 3).reshape(-1, head_size)
    extra = jnp.zeros((16, lane), jnp.bfloat16)
    extra = extra.at[0, :rows].set(segments.astype(jnp.bfloat16))
    packed = jnp.concatenate([body, extra], axis=0)
    body_rows = body.shape[0]
    gathered = lax.all_gather(packed, "tensor", axis=0, tiled=False)

    my_first = lax.axis_index("tensor") * rows
    query_pos = my_first + jnp.arange(rows)
    query_bound = bound_of(segments, limits)
    info = jnp.stack([segments, query_pos, query_bound], axis=1).astype(jnp.int32)

    pieces = []
    for h in range(kv_heads):
        out_h = attention_head(query_rows, gathered, info, h, body_rows, kv_heads, head_size)
        pieces.append(from_behind(out_h, "section", 1))
    return jnp.concatenate(pieces, axis=1)[None]


def solution(mesh):
    in_specs = (
        P("section", ("dp", "tensor"), None),
        P("section", ("dp", "tensor"), None, None),
        P("section", ("dp", "tensor")),
        P("section", "dp"),
    )
    out_specs = P("section", ("dp", "tensor"), None)
    return jax.shard_map(attend, mesh=mesh, in_specs=in_specs, out_specs=out_specs, check_vma=False)
```

```python
import functools
import math

import jax
import jax.numpy as jnp
from jax import lax
from jax.experimental import pallas as pl
from jax.sharding import PartitionSpec as P


def from_behind(block, axis, distance):
    devices = range(lax.axis_size(axis))
    route = [((i - distance) % len(devices), i) for i in devices]
    return lax.ppermute(block, axis, route)


def bound_of(segments, limits):
    levels = jnp.arange(limits.shape[0])
    return jnp.sum(jnp.where(segments[:, None] == levels[None, :], limits[None, :], 0), axis=1)


def attention_kernel(q_ref, g_ref, s_ref, i_ref, o_ref, *, groups, head_size, scale):
    parts = g_ref.shape[0]
    span = parts * head_size
    k = g_ref[:, :head_size, :].reshape(span, head_size)
    v = g_ref[:, head_size:, :].reshape(span, head_size)
    own = i_ref[:, 0:1]
    place = i_ref[:, 1:2]
    reach = i_ref[:, 2:3]
    blocks = []
    for p in range(parts):
        key_seg = s_ref[p, 0:1, :].astype(jnp.int32)
        key_pos = p * head_size + lax.broadcasted_iota(jnp.int32, (1, head_size), 1)
        seen = (own == key_seg) & ((key_pos <= place) | (key_pos <= reach))
        blocks.append(jnp.where(seen, 0.0, -1e30).astype(jnp.float32))
    bias = jnp.concatenate(blocks, axis=1)
    for g in range(groups):
        qg = q_ref[:, g * head_size : (g + 1) * head_size]
        s = lax.dot_general(qg, k, (((1,), (1,)), ((), ())), preferred_element_type=jnp.float32)
        s = s * scale + bias
        m = jnp.max(s, axis=1, keepdims=True)
        w = jnp.exp(s - m)
        total = jnp.sum(w, axis=1, keepdims=True)
        pv = jnp.dot(w.astype(jnp.bfloat16), v, preferred_element_type=jnp.float32)
        o_ref[:, g * head_size : (g + 1) * head_size] = (pv / total).astype(o_ref.dtype)


def attention_head(q, gathered, info, first, count, id_row, kv_heads, head_size):
    rows, width = q.shape
    groups = count
    block = groups * head_size
    head = first // (width // head_size // kv_heads)
    kernel = functools.partial(
        attention_kernel, groups=groups, head_size=head_size, scale=1.0 / math.sqrt(head_size)
    )
    return pl.pallas_call(
        kernel,
        grid=(1,),
        in_specs=[
            pl.BlockSpec((rows, block), lambda i: (0, first // count)),
            pl.BlockSpec((gathered.shape[0], 2 * head_size, gathered.shape[2]), lambda i: (0, head, 0)),
            pl.BlockSpec((gathered.shape[0], 16, gathered.shape[2]), lambda i: (0, id_row // 16, 0)),
            pl.BlockSpec(info.shape, lambda i: (0, 0)),
        ],
        out_specs=pl.BlockSpec((rows, block), lambda i: (0, 0)),
        out_shape=jax.ShapeDtypeStruct((rows, block), jnp.bfloat16),
    )(q, gathered, gathered, info)


def chunk_plan(heads, kv_heads):
    groups = heads // kv_heads
    plan = [(0, groups // 2), (groups // 2, groups // 2)]
    plan += [(h * groups, groups) for h in range(1, kv_heads)]
    return plan


def attend(queries, keys_values, segment_ids, bounds):
    query_rows = queries[0]
    pairs = keys_values[0]
    segments = segment_ids[0]
    limits = bounds[0]
    rows = query_rows.shape[0]
    kv_heads = pairs.shape[1]
    width = pairs.shape[2]
    head_size = width // 2
    lane = 128

    body = pairs.reshape(rows, kv_heads, 2, head_size).transpose(1, 2, 0, 3).reshape(-1, head_size)
    extra = jnp.zeros((16, lane), jnp.bfloat16)
    extra = extra.at[0, :rows].set(segments.astype(jnp.bfloat16))
    packed = jnp.concatenate([body, extra], axis=0)
    body_rows = body.shape[0]
    gathered = lax.all_gather(packed, "tensor", axis=0, tiled=False)

    my_first = lax.axis_index("tensor") * rows
    query_pos = my_first + jnp.arange(rows)
    query_bound = bound_of(segments, limits)
    info = jnp.stack([segments, query_pos, query_bound], axis=1).astype(jnp.int32)

    pieces = []
    for first, count in chunk_plan(query_rows.shape[1] // head_size, kv_heads):
        out_c = attention_head(query_rows, gathered, info, first, count, body_rows, kv_heads, head_size)
        pieces.append(from_behind(out_c, "section", 1))
    return jnp.concatenate(pieces, axis=1)[None]


def solution(mesh):
    in_specs = (
        P("section", ("dp", "tensor"), None),
        P("section", ("dp", "tensor"), None, None),
        P("section", ("dp", "tensor")),
        P("section", "dp"),
    )
    out_specs = P("section", ("dp", "tensor"), None)
    return jax.shard_map(attend, mesh=mesh, in_specs=in_specs, out_specs=out_specs, check_vma=False)
```

```python
import functools
import math

import jax
import jax.numpy as jnp
from jax import lax
from jax.experimental import pallas as pl
from jax.sharding import PartitionSpec as P


def bound_of(segments, limits):
    levels = jnp.arange(limits.shape[0])
    return jnp.sum(jnp.where(segments[:, None] == levels[None, :], limits[None, :], 0), axis=1)


def attention_kernel(q_ref, g_ref, s_ref, i_ref, o_ref, *, groups, head_size, scale):
    parts = g_ref.shape[0]
    span = parts * head_size
    k = g_ref[:, :head_size, :].reshape(span, head_size)
    v = g_ref[:, head_size:, :].reshape(span, head_size)
    own = i_ref[:, 0:1]
    place = i_ref[:, 1:2]
    reach = i_ref[:, 2:3]
    blocks = []
    for p in range(parts):
        key_seg = s_ref[p, 0:1, :].astype(jnp.int32)
        key_pos = p * head_size + lax.broadcasted_iota(jnp.int32, (1, head_size), 1)
        seen = (own == key_seg) & ((key_pos <= place) | (key_pos <= reach))
        blocks.append(jnp.where(seen, 0.0, -1e30).astype(jnp.float32))
    bias = jnp.concatenate(blocks, axis=1)
    for g in range(groups):
        qg = q_ref[:, g * head_size : (g + 1) * head_size]
        s = lax.dot_general(qg, k, (((1,), (1,)), ((), ())), preferred_element_type=jnp.float32)
        s = s * scale + bias
        m = jnp.max(s, axis=1, keepdims=True)
        w = jnp.exp(s - m)
        total = jnp.sum(w, axis=1, keepdims=True)
        pv = jnp.dot(w.astype(jnp.bfloat16), v, preferred_element_type=jnp.float32)
        o_ref[:, g * head_size : (g + 1) * head_size] = (pv / total).astype(o_ref.dtype)


def attention_head(q, gathered, info, first, count, id_row, kv_heads, head_size):
    rows, width = q.shape
    per_kv = width // head_size // kv_heads
    groups = min(count, per_kv)
    steps = count // groups
    block = groups * head_size
    kv_first = first // per_kv
    kernel = functools.partial(
        attention_kernel, groups=groups, head_size=head_size, scale=1.0 / math.sqrt(head_size)
    )
    return pl.pallas_call(
        kernel,
        grid=(steps,),
        in_specs=[
            pl.BlockSpec((rows, block), lambda i: (0, first // groups + i)),
            pl.BlockSpec(
                (gathered.shape[0], 2 * head_size, gathered.shape[2]),
                lambda i: (0, kv_first + i * groups // per_kv, 0),
            ),
            pl.BlockSpec((gathered.shape[0], 16, gathered.shape[2]), lambda i: (0, id_row // 16, 0)),
            pl.BlockSpec(info.shape, lambda i: (0, 0)),
        ],
        out_specs=pl.BlockSpec((rows, block), lambda i: (0, i)),
        out_shape=jax.ShapeDtypeStruct((rows, count * head_size), jnp.bfloat16),
    )(q, gathered, gathered, info)


def relay_routes(sections, parts):
    ring = 2 * parts
    quarter = parts // 2

    def at(y, z):
        high, t = divmod(z % ring, parts)
        return (2 * y + high) * parts + t

    routes = {"up1": [], "up2": [], "dn1": [], "dn2": []}
    for section in range(sections):
        y, high = divmod(section, 2)
        for t in range(parts):
            z = high * parts + t
            src = section * parts + t
            dst = ((section + 1) % sections) * parts + t
            ahead, behind = at(y, z + quarter), at(y, z - quarter)
            routes["up1"].append((src, ahead))
            routes["up2"].append((ahead, dst))
            routes["dn1"].append((src, behind))
            routes["dn2"].append((behind, dst))
    return routes


def chunk_plan(heads, kv_heads):
    groups = heads // kv_heads
    return [(0, groups), (groups, heads - groups)]


def attend(queries, keys_values, segment_ids, bounds):
    query_rows = queries[0]
    pairs = keys_values[0]
    segments = segment_ids[0]
    limits = bounds[0]
    rows = query_rows.shape[0]
    kv_heads = pairs.shape[1]
    width = pairs.shape[2]
    head_size = width // 2
    lane = 128
    tensor_size = lax.axis_size("tensor")

    body = pairs.reshape(rows, kv_heads, 2, head_size).transpose(1, 2, 0, 3).reshape(-1, head_size)
    extra = jnp.zeros((16, lane), jnp.bfloat16)
    extra = extra.at[0, :rows].set(segments.astype(jnp.bfloat16))
    packed = jnp.concatenate([body, extra], axis=0)
    body_rows = body.shape[0]
    gathered = lax.all_gather(packed, "tensor", axis=0, tiled=False)

    my_first = lax.axis_index("tensor") * rows
    query_pos = my_first + jnp.arange(rows)
    query_bound = bound_of(segments, limits)
    info = jnp.stack([segments, query_pos, query_bound], axis=1).astype(jnp.int32)

    routes = relay_routes(lax.axis_size("section"), tensor_size)
    axes = ("section", "tensor")
    pieces = []
    for first, count in chunk_plan(query_rows.shape[1] // head_size, kv_heads):
        out_c = attention_head(query_rows, gathered, info, first, count, body_rows, kv_heads, head_size)
        split = out_c.shape[1] // 2
        up = lax.ppermute(out_c[:, :split], axes, routes["up1"])
        down = lax.ppermute(out_c[:, split:], axes, routes["dn1"])
        up = lax.ppermute(up, axes, routes["up2"])
        down = lax.ppermute(down, axes, routes["dn2"])
        pieces += [up, down]
    return jnp.concatenate(pieces, axis=1)[None]


def solution(mesh):
    in_specs = (
        P("section", ("dp", "tensor"), None),
        P("section", ("dp", "tensor"), None, None),
        P("section", ("dp", "tensor")),
        P("section", "dp"),
    )
    out_specs = P("section", ("dp", "tensor"), None)
    return jax.shard_map(attend, mesh=mesh, in_specs=in_specs, out_specs=out_specs, check_vma=False)
```

```python
import functools
import math

import jax
import jax.numpy as jnp
from jax import lax
from jax.experimental import pallas as pl
from jax.sharding import PartitionSpec as P


def from_behind(block, axis, distance):
    devices = range(lax.axis_size(axis))
    route = [((i - distance) % len(devices), i) for i in devices]
    return lax.ppermute(block, axis, route)


def bound_of(segments, limits):
    levels = jnp.arange(limits.shape[0])
    return jnp.sum(jnp.where(segments[:, None] == levels[None, :], limits[None, :], 0), axis=1)


def attention_kernel(q_ref, g_ref, s_ref, i_ref, o_ref, *, groups, head_size, scale):
    parts = g_ref.shape[0]
    span = parts * head_size
    k = g_ref[:, :head_size, :].reshape(span, head_size)
    v = g_ref[:, head_size:, :].reshape(span, head_size)
    own = i_ref[:, 0:1]
    place = i_ref[:, 1:2]
    reach = i_ref[:, 2:3]
    blocks = []
    for p in range(parts):
        key_seg = s_ref[p, 0:1, :].astype(jnp.int32)
        key_pos = p * head_size + lax.broadcasted_iota(jnp.int32, (1, head_size), 1)
        seen = (own == key_seg) & ((key_pos <= place) | (key_pos <= reach))
        blocks.append(jnp.where(seen, 0.0, -1e30).astype(jnp.float32))
    bias = jnp.concatenate(blocks, axis=1)
    for g in range(groups):
        qg = q_ref[:, g * head_size : (g + 1) * head_size]
        s = lax.dot_general(qg, k, (((1,), (1,)), ((), ())), preferred_element_type=jnp.float32)
        s = s * scale + bias
        m = jnp.max(s, axis=1, keepdims=True)
        w = jnp.exp(s - m)
        total = jnp.sum(w, axis=1, keepdims=True)
        pv = jnp.dot(w.astype(jnp.bfloat16), v, preferred_element_type=jnp.float32)
        o_ref[:, g * head_size : (g + 1) * head_size] = (pv / total).astype(o_ref.dtype)


def attention_head(q, gathered, info, first, count, id_row, kv_heads, head_size):
    rows, width = q.shape
    per_kv = width // head_size // kv_heads
    groups = min(count, per_kv)
    steps = count // groups
    block = groups * head_size
    kv_first = first // per_kv
    kernel = functools.partial(
        attention_kernel, groups=groups, head_size=head_size, scale=1.0 / math.sqrt(head_size)
    )
    return pl.pallas_call(
        kernel,
        grid=(steps,),
        in_specs=[
            pl.BlockSpec((rows, block), lambda i: (0, first // groups + i)),
            pl.BlockSpec(
                (gathered.shape[0], 2 * head_size, gathered.shape[2]),
                lambda i: (0, kv_first + i * groups // per_kv, 0),
            ),
            pl.BlockSpec((gathered.shape[0], 16, gathered.shape[2]), lambda i: (0, id_row // 16, 0)),
            pl.BlockSpec(info.shape, lambda i: (0, 0)),
        ],
        out_specs=pl.BlockSpec((rows, block), lambda i: (0, i)),
        out_shape=jax.ShapeDtypeStruct((rows, count * head_size), jnp.bfloat16),
    )(q, gathered, gathered, info)


def chunk_plan(heads, kv_heads):
    groups = heads // kv_heads
    return [(0, groups), (groups, heads - groups)]


def attend(queries, keys_values, segment_ids, bounds):
    query_rows = queries[0]
    pairs = keys_values[0]
    segments = segment_ids[0]
    limits = bounds[0]
    rows = query_rows.shape[0]
    kv_heads = pairs.shape[1]
    width = pairs.shape[2]
    head_size = width // 2
    lane = 128

    body = pairs.reshape(rows, kv_heads, 2, head_size).transpose(1, 2, 0, 3).reshape(-1, head_size)
    extra = jnp.pad(segments.astype(jnp.bfloat16)[None, :], ((0, 15), (0, lane - rows)))
    packed = jnp.concatenate([body, extra], axis=0)
    body_rows = body.shape[0]
    gathered = lax.all_gather(packed, "tensor", axis=0, tiled=False)

    my_first = lax.axis_index("tensor") * rows
    query_pos = my_first + jnp.arange(rows)
    query_bound = bound_of(segments, limits)
    info = jnp.stack([segments, query_pos, query_bound], axis=1).astype(jnp.int32)

    pieces = []
    for first, count in chunk_plan(query_rows.shape[1] // head_size, kv_heads):
        out_c = attention_head(query_rows, gathered, info, first, count, body_rows, kv_heads, head_size)
        pieces.append(from_behind(out_c, "section", 1))
    return jnp.concatenate(pieces, axis=1)[None]


def solution(mesh):
    in_specs = (
        P("section", ("dp", "tensor"), None),
        P("section", ("dp", "tensor"), None, None),
        P("section", ("dp", "tensor")),
        P("section", "dp"),
    )
    out_specs = P("section", ("dp", "tensor"), None)
    return jax.shard_map(attend, mesh=mesh, in_specs=in_specs, out_specs=out_specs, check_vma=False)
```
